256 devices in a mesh: pair: 32 (over x, z), vir: 8 (over y, core).
Axes of the slice: x: 4, y: 4, z: 8, core: 2. Of those that a mesh axis runs over, the one named last changes fastest.
Arguments:
- amplitudes: float32 [24576, 4096], P(('pair', 'vir')), may hold values from -6 to 6
- integrals: float32 [1536, 1536], P('vir'), may hold values from -0.15625 to 0.15625
- tile_owner: int32 [24576], P(('pair', 'vir')), may hold values from 0 to 31, as said below
- tile_key: int32 [24576], P(('pair', 'vir')), may hold values from 0 to 575
Outputs:
- residual: float32 [24576, 4096], P(('pair', 'vir'))
The draws below stay inside these ranges and needn't reach their ends.
Inputs may be any that keep to these rules, and one draw needn't show every extreme that they name: `tile_owner`: among the 96 tiles of one device no owner is named more than 6 times; one owner, the same for every device, is named exactly 6 times by each device.
All inputs are finite; a program needn't handle non-finite values.
Results may differ from the reference program's by a relative error of at most 0.0003.
Values sent between devices are 32-bit elements; how exact they have to be, the bound alone decides.
No kernel may reach another device: no remote copies, remote signals or barrier semaphores. Data moves between devices by JAX's collectives and lax.ppermute only.
A program may use at most 128 MiB of HBM per device.

```python
import jax
import jax.numpy as jnp
from jax import lax

TS = 64
NS = 24
ROWSETS_DEV = 24
TILES_DEV = 96
OWNERS = 32
GROUPS = 8
CAP = 6
TILES = 24576


def draw_tile_owner(key, part):
    device_count = TILES // TILES_DEV
    hottest = jax.random.randint(jax.random.fold_in(key, 11), (), 0, OWNERS)
    position = jnp.arange(TILES_DEV, dtype=jnp.int32)

    def per_device(dev_key):
        offset = jax.random.randint(dev_key, (), 0, OWNERS - 1)
        others = (position - CAP + offset) % (OWNERS - 1)
        others = others + (others >= hottest).astype(jnp.int32)
        owners = jnp.where(position < CAP, hottest, others)
        order = jax.random.permutation(jax.random.fold_in(dev_key, 7), TILES_DEV)
        return owners[order]
    dev_keys = jax.random.split(jax.random.fold_in(key, 23), device_count)
    return jax.vmap(per_device)(dev_keys).reshape(TILES).astype(jnp.int32)


def plant(drawn, rng, least, high):
    spot = [jax.random.randint(jax.random.fold_in(rng, axis), (), 0, length) for axis, length in enumerate(drawn.shape)]
    longest = drawn.shape.index(max(drawn.shape))
    neighbour = spot[:longest] + [(spot[longest] + 1) % drawn.shape[longest]] + spot[longest + 1:]
    return drawn.at[tuple(spot)].set(least).at[tuple(neighbour)].set(high)


def level_of(stream_key, extent, pieces, smallest, largest):
    loudness = 1.0
    for dim, parts in pieces:
        draws = jax.random.uniform(jax.random.fold_in(jax.random.fold_in(stream_key, 6), dim), (parts,), jnp.float32, smallest / len(pieces), largest / len(pieces))
        loudness = loudness * jnp.repeat(jnp.exp(draws), extent[dim] // parts).reshape((-1,) + (1,) * (len(extent) - 1 - dim))
    return loudness


def centred(stream_key, shape, deviation, bound, shards=(), kind=jnp.bfloat16):
    result = jax.random.normal(stream_key, shape, jnp.float32) * deviation
    if len(shards) > 0:
        result = level_of(stream_key, shape, shards, -0.22, 0.18) * result
    return jnp.clip(result, min=-bound, max=bound).astype(kind)


def setup_inputs(seed: int = 0) -> dict:
    key_of = jax.random.split(jax.random.key(seed), 5)
    return {
        "amplitudes": centred(key_of[0], (TILES, TS * TS), 1.0, 6.0, ((0, 256),), jnp.float32),
        "integrals": centred(key_of[1], (NS * TS, NS * TS), (NS * TS) ** -0.5, 0.15625, ((0, 8),), jnp.float32),
        "tile_owner": draw_tile_owner(jax.random.fold_in(key_of[4], 71), 0),
        "tile_key": plant(jax.random.randint(key_of[3], (TILES,), 0, ROWSETS_DEV * NS), jax.random.fold_in(key_of[3], 1), 0, (ROWSETS_DEV * NS) - 1).astype(jnp.int32),
    }


def regroup(values):
    shaped = values.reshape((OWNERS, GROUPS, TILES_DEV) + values.shape[1:])
    shaped = jnp.moveaxis(shaped, 1, 0)
    return shaped.reshape((GROUPS, OWNERS * TILES_DEV) + values.shape[1:])


def reference(amplitudes, integrals, tile_owner, tile_key):
    amp_groups = regroup(amplitudes).reshape(GROUPS, OWNERS * TILES_DEV, TS, TS)
    owner_groups = regroup(tile_owner)
    key_groups = regroup(tile_key)
    column_tables = integrals.reshape(NS * TS, NS, TS)

    def one_group(packed):
        amp_group, owner_group, key_group = packed
        row_block = (owner_group * ROWSETS_DEV + key_group // NS).astype(jnp.int32)
        col_block = (key_group % NS).astype(jnp.int32)
        blocked = jnp.zeros((OWNERS * ROWSETS_DEV, TS, NS, TS), jnp.float32)
        blocked = blocked.at[row_block, :, col_block, :].add(amp_group)
        blocked = blocked.reshape(OWNERS * ROWSETS_DEV, TS, NS * TS)

        def one_batch(batch):
            rows_here, cols_here = batch
            left_rows = blocked[rows_here]
            right_cols = column_tables[:, cols_here, :]
            return jnp.einsum("bik,kbj->bij", left_rows, right_cols, precision=lax.Precision.HIGHEST)

        batches = (row_block.reshape(OWNERS, TILES_DEV), col_block.reshape(OWNERS, TILES_DEV))
        return lax.map(one_batch, batches).reshape(OWNERS * TILES_DEV, TS * TS)

    residual_groups = lax.map(one_group, (amp_groups, owner_groups, key_groups))
    shaped = residual_groups.reshape(GROUPS, OWNERS, TILES_DEV, TS * TS)
    return jnp.moveaxis(shaped, 0, 1).reshape(OWNERS * GROUPS * TILES_DEV, TS * TS)
```

```python
import jax
import jax.numpy as jnp
from jax import lax
from jax.sharding import PartitionSpec as P

TS = 64
NS = 24
ROWSETS_DEV = 24

_WINDOW = lax.ScatterDimensionNumbers(
    update_window_dims=(1, 2), inserted_window_dims=(), scatter_dims_to_operand_dims=(0, 1)
)
_TAKE = lax.GatherDimensionNumbers(
    offset_dims=(1, 2), collapsed_slice_dims=(), start_index_map=(0, 1)
)


def per_device(amplitudes, integrals, tile_owner, tile_key):
    owner_count = lax.axis_size("pair")
    capacity = max(2, 2 * amplitudes.shape[0] // owner_count)
    picked = (tile_owner[:, None] == jnp.arange(owner_count, dtype=jnp.int32)[None, :]).astype(
        jnp.int32
    )
    before = jnp.cumsum(picked, axis=0) - picked
    slot_index = jnp.sum(before * picked, axis=1)
    send_tiles = (
        jnp.zeros((owner_count, capacity, TS * TS), jnp.float32)
        .at[tile_owner, slot_index]
        .set(amplitudes)
    )
    send_keys = (
        jnp.zeros((owner_count, capacity), jnp.int32).at[tile_owner, slot_index].set(tile_key)
    )
    recv_tiles, recv_keys = (
        lax.all_to_all(send_tiles, "pair", split_axis=0, concat_axis=0, tiled=True),
        lax.all_to_all(send_keys, "pair", split_axis=0, concat_axis=0, tiled=True),
    )
    arrived = recv_tiles.reshape(owner_count * capacity, TS, TS)
    flat_keys = recv_keys.reshape(owner_count * capacity)
    row_block = flat_keys // NS
    col_block = flat_keys % NS
    corner = jnp.stack([row_block * TS, col_block * TS], axis=1)
    blocked = lax.scatter_add(
        jnp.zeros((ROWSETS_DEV * TS, NS * TS), jnp.float32),
        corner,
        arrived,
        _WINDOW,
        indices_are_sorted=False,
        unique_indices=False,
        mode=lax.GatherScatterMode.PROMISE_IN_BOUNDS,
    )
    product = jnp.dot(
        blocked,
        lax.all_gather(integrals, "vir", axis=0, tiled=True),
        precision=lax.Precision.HIGH,
        preferred_element_type=jnp.float32,
    )
    answers = lax.gather(
        product,
        corner,
        _TAKE,
        slice_sizes=(TS, TS),
        indices_are_sorted=False,
        unique_indices=False,
        mode=lax.GatherScatterMode.PROMISE_IN_BOUNDS,
    )
    answers = answers.reshape(owner_count, capacity, TS * TS)
    returned = lax.all_to_all(answers, "pair", split_axis=0, concat_axis=0, tiled=True)
    return returned[tile_owner, slot_index]


def solution(mesh):
    placed = (P(("pair", "vir"), None), P("vir", None), P(("pair", "vir")), P(("pair", "vir")))
    return jax.shard_map(
        per_device, mesh=mesh, in_specs=placed, out_specs=P(("pair", "vir"), None), check_vma=False
    )
```

```python
import jax
import jax.numpy as jnp
from jax import lax
from jax.sharding import PartitionSpec as P

TS = 64
NS = 24
ROWSETS_DEV = 24


def per_device(amplitudes, integrals, tile_owner, tile_key):
    owner_count = lax.axis_size("pair")
    capacity = max(2, 2 * amplitudes.shape[0] // owner_count)
    picked = (tile_owner[:, None] == jnp.arange(owner_count, dtype=jnp.int32)[None, :]).astype(
        jnp.int32
    )
    before = jnp.cumsum(picked, axis=0) - picked
    slot_index = jnp.sum(before * picked, axis=1)
    send_tiles = (
        jnp.zeros((owner_count, capacity, TS * TS), jnp.float32)
        .at[tile_owner, slot_index]
        .set(amplitudes)
    )
    send_keys = (
        jnp.zeros((owner_count, capacity), jnp.int32).at[tile_owner, slot_index].set(tile_key)
    )
    recv_tiles, recv_keys = (
        lax.all_to_all(send_tiles, "pair", split_axis=0, concat_axis=0, tiled=True),
        lax.all_to_all(send_keys, "pair", split_axis=0, concat_axis=0, tiled=True),
    )
    arrived = recv_tiles.reshape(owner_count * capacity, TS * TS)
    flat_keys = recv_keys.reshape(owner_count * capacity)
    row_block = flat_keys // NS
    col_block = flat_keys % NS
    places = jnp.arange(ROWSETS_DEV * NS, dtype=jnp.int32)
    chooser = (places[:, None] == flat_keys[None, :]).astype(jnp.float32)
    stacked = jnp.dot(
        chooser, arrived, precision=lax.Precision.HIGHEST, preferred_element_type=jnp.float32
    )
    blocked = stacked.reshape(ROWSETS_DEV, NS, TS, TS).transpose(0, 2, 1, 3)
    blocked = blocked.reshape(ROWSETS_DEV * TS, NS * TS)
    product = jnp.dot(
        blocked,
        lax.all_gather(integrals, "vir", axis=0, tiled=True),
        precision=lax.Precision.HIGH,
        preferred_element_type=jnp.float32,
    )
    product = product.reshape(ROWSETS_DEV, TS, NS, TS)
    answers = product[row_block, :, col_block, :].reshape(owner_count, capacity, TS * TS)
    returned = lax.all_to_all(answers, "pair", split_axis=0, concat_axis=0, tiled=True)
    return returned[tile_owner, slot_index]


def solution(mesh):
    placed = (P(("pair", "vir"), None), P("vir", None), P(("pair", "vir")), P(("pair", "vir")))
    return jax.shard_map(
        per_device, mesh=mesh, in_specs=placed, out_specs=P(("pair", "vir"), None), check_vma=False
    )
```

```python
import jax
import jax.numpy as jnp
from jax import lax
from jax.sharding import PartitionSpec as P

TS = 64
NS = 24
ROWSETS_DEV = 24


def per_device(amplitudes, integrals, tile_owner, tile_key):
    owner_count = lax.axis_size("pair")
    capacity = max(2, 2 * amplitudes.shape[0] // owner_count)
    picked = (tile_owner[:, None] == jnp.arange(owner_count, dtype=jnp.int32)[None, :]).astype(
        jnp.int32
    )
    before = jnp.cumsum(picked, axis=0) - picked
    slot_index = jnp.sum(before * picked, axis=1)
    slots = jnp.arange(owner_count * capacity, dtype=jnp.int32)
    packer = (slots[:, None] == (tile_owner * capacity + slot_index)[None, :]).astype(jnp.float32)
    key_lanes = jnp.broadcast_to(tile_key.astype(jnp.float32)[:, None], (tile_key.shape[0], 128))
    payload = jnp.concatenate([amplitudes, key_lanes], axis=1)
    send = jnp.dot(
        packer, payload, precision=lax.Precision.HIGHEST, preferred_element_type=jnp.float32
    ).reshape(owner_count, capacity, TS * TS + 128)
    recv = lax.all_to_all(send, "pair", split_axis=0, concat_axis=0, tiled=True)
    recv = recv.reshape(owner_count * capacity, TS * TS + 128)
    arrived = recv[:, : TS * TS]
    flat_keys = recv[:, TS * TS].astype(jnp.int32)
    row_block = flat_keys // NS
    col_block = flat_keys % NS
    places = jnp.arange(ROWSETS_DEV * NS, dtype=jnp.int32)
    chooser = (places[:, None] == flat_keys[None, :]).astype(jnp.float32)
    stacked = jnp.dot(
        chooser, arrived, precision=lax.Precision.HIGHEST, preferred_element_type=jnp.float32
    )
    blocked = stacked.reshape(ROWSETS_DEV, NS, TS, TS).transpose(0, 2, 1, 3)
    blocked = blocked.reshape(ROWSETS_DEV * TS, NS * TS)
    product = jnp.dot(
        blocked,
        lax.all_gather(integrals, "vir", axis=0, tiled=True),
        precision=lax.Precision.HIGH,
        preferred_element_type=jnp.float32,
    )
    product = product.reshape(ROWSETS_DEV, TS, NS, TS)
    answers = product[row_block, :, col_block, :].reshape(owner_count, capacity, TS * TS)
    returned = lax.all_to_all(answers, "pair", split_axis=0, concat_axis=0, tiled=True)
    returned = returned.reshape(owner_count * capacity, TS * TS)
    return jnp.dot(
        packer.T, returned, precision=lax.Precision.HIGHEST, preferred_element_type=jnp.float32
    )


def solution(mesh):
    placed = (P(("pair", "vir"), None), P("vir", None), P(("pair", "vir")), P(("pair", "vir")))
    return jax.shard_map(
        per_device, mesh=mesh, in_specs=placed, out_specs=P(("pair", "vir"), None), check_vma=False
    )
```

```python
import jax
import jax.numpy as jnp
from jax import lax
from jax.sharding import PartitionSpec as P

TS = 64
NS = 24
ROWSETS_DEV = 24


def slots_of(owners, count):
    picked = (owners[..., :, None] == jnp.arange(count, dtype=jnp.int32)).astype(jnp.int32)
    before = jnp.cumsum(picked, axis=-2) - picked
    return jnp.sum(before * picked, axis=-1)


def per_device(amplitudes, integrals, tile_owner, tile_key):
    owner_count = lax.axis_size("pair")
    capacity = max(2, 2 * amplitudes.shape[0] // owner_count)
    slot_index = slots_of(tile_owner, owner_count)
    owners_all = lax.all_gather(tile_owner, "pair", axis=0)
    keys_all = lax.all_gather(tile_key, "pair", axis=0)
    me = lax.axis_index("pair")
    slots_all = slots_of(owners_all, owner_count)
    mine = owners_all == me
    hits = mine[:, :, None] & (slots_all[:, :, None] == jnp.arange(capacity, dtype=jnp.int32))
    flat_keys = jnp.sum(jnp.where(hits, keys_all[:, :, None], 0), axis=1).reshape(-1)
    slots = jnp.arange(owner_count * capacity, dtype=jnp.int32)
    packer = (slots[:, None] == (tile_owner * capacity + slot_index)[None, :]).astype(jnp.float32)
    send = jnp.dot(
        packer, amplitudes, precision=lax.Precision.HIGHEST, preferred_element_type=jnp.float32
    ).reshape(owner_count, capacity, TS * TS)
    recv = lax.all_to_all(send, "pair", split_axis=0, concat_axis=0, tiled=True)
    arrived = recv.reshape(owner_count * capacity, TS * TS)
    row_block = flat_keys // NS
    col_block = flat_keys % NS
    places = jnp.arange(ROWSETS_DEV * NS, dtype=jnp.int32)
    chooser = (places[:, None] == flat_keys[None, :]).astype(jnp.float32)
    stacked = jnp.dot(
        chooser, arrived, precision=lax.Precision.HIGHEST, preferred_element_type=jnp.float32
    )
    blocked = stacked.reshape(ROWSETS_DEV, NS, TS, TS).transpose(0, 2, 1, 3)
    blocked = blocked.reshape(ROWSETS_DEV * TS, NS * TS)
    product = jnp.dot(
        blocked,
        lax.all_gather(integrals, "vir", axis=0, tiled=True),
        precision=lax.Precision.HIGH,
        preferred_element_type=jnp.float32,
    )
    product = product.reshape(ROWSETS_DEV, TS, NS, TS)
    answers = product[row_block, :, col_block, :].reshape(owner_count, capacity, TS * TS)
    returned = lax.all_to_all(answers, "pair", split_axis=0, concat_axis=0, tiled=True)
    returned = returned.reshape(owner_count * capacity, TS * TS)
    return jnp.dot(
        packer.T, returned, precision=lax.Precision.HIGHEST, preferred_element_type=jnp.float32
    )


def solution(mesh):
    placed = (P(("pair", "vir"), None), P("vir", None), P(("pair", "vir")), P(("pair", "vir")))
    return jax.shard_map(
        per_device, mesh=mesh, in_specs=placed, out_specs=P(("pair", "vir"), None), check_vma=False
    )
```

```python
import jax
import jax.numpy as jnp
from jax import lax
from jax.sharding import PartitionSpec as P

TS = 64
NS = 24
ROWSETS_DEV = 24


def per_device(amplitudes, integrals, tile_owner, tile_key):
    owner_count = lax.axis_size("pair")
    capacity = max(2, 2 * amplitudes.shape[0] // owner_count)
    picked = (tile_owner[:, None] == jnp.arange(owner_count, dtype=jnp.int32)[None, :]).astype(
        jnp.int32
    )
    before = jnp.cumsum(picked, axis=0) - picked
    slot_index = jnp.sum(before * picked, axis=1)
    slots = jnp.arange(owner_count * capacity, dtype=jnp.int32)
    packer = (slots[:, None] == (tile_owner * capacity + slot_index)[None, :]).astype(jnp.float32)
    send = jnp.dot(
        packer, amplitudes, precision=lax.Precision.HIGHEST, preferred_element_type=jnp.float32
    ).reshape(owner_count, capacity, TS * TS)
    send_keys = (
        jnp.zeros((owner_count, capacity), jnp.int32).at[tile_owner, slot_index].set(tile_key)
    )
    recv = lax.all_to_all(send, "pair", split_axis=0, concat_axis=0, tiled=True)
    recv_keys = lax.all_to_all(send_keys, "pair", split_axis=0, concat_axis=0, tiled=True)
    arrived = recv.reshape(owner_count * capacity, TS * TS)
    flat_keys = recv_keys.reshape(owner_count * capacity)
    row_block = flat_keys // NS
    col_block = flat_keys % NS
    places = jnp.arange(ROWSETS_DEV * NS, dtype=jnp.int32)
    chooser = (places[:, None] == flat_keys[None, :]).astype(jnp.float32)
    stacked = jnp.dot(
        chooser, arrived, precision=lax.Precision.HIGHEST, preferred_element_type=jnp.float32
    )
    blocked = stacked.reshape(ROWSETS_DEV, NS, TS, TS).transpose(0, 2, 1, 3)
    blocked = blocked.reshape(ROWSETS_DEV * TS, NS * TS)
    product = jnp.dot(
        blocked,
        lax.all_gather(integrals, "vir", axis=0, tiled=True),
        precision=lax.Precision.HIGH,
        preferred_element_type=jnp.float32,
    )
    product = product.reshape(ROWSETS_DEV, TS, NS, TS)
    answers = product[row_block, :, col_block, :].reshape(owner_count, capacity, TS * TS)
    returned = lax.all_to_all(answers, "pair", split_axis=0, concat_axis=0, tiled=True)
    returned = returned.reshape(owner_count * capacity, TS * TS)
    return jnp.dot(
        packer.T, returned, precision=lax.Precision.HIGHEST, preferred_element_type=jnp.float32
    )


def solution(mesh):
    placed = (P(("pair", "vir"), None), P("vir", None), P(("pair", "vir")), P(("pair", "vir")))
    return jax.shard_map(
        per_device, mesh=mesh, in_specs=placed, out_specs=P(("pair", "vir"), None), check_vma=False
    )
```

```python
import jax
import jax.numpy as jnp
from jax import lax
from jax.sharding import PartitionSpec as P

TS = 64
NS = 24
ROWSETS_DEV = 24


def per_device(amplitudes, integrals, tile_owner, tile_key):
    owner_count = lax.axis_size("pair")
    capacity = max(2, 2 * amplitudes.shape[0] // owner_count)
    picked = (tile_owner[:, None] == jnp.arange(owner_count, dtype=jnp.int32)[None, :]).astype(
        jnp.int32
    )
    before = jnp.cumsum(picked, axis=0) - picked
    slot_index = jnp.sum(before * picked, axis=1)
    slots = jnp.arange(owner_count * capacity, dtype=jnp.int32)
    packer = (slots[:, None] == (tile_owner * capacity + slot_index)[None, :]).astype(jnp.float32)
    send = jnp.dot(
        packer, amplitudes, precision=lax.Precision.HIGHEST, preferred_element_type=jnp.float32
    ).reshape(owner_count, capacity, TS * TS)
    send_keys = (
        jnp.zeros((owner_count, capacity), jnp.int32).at[tile_owner, slot_index].set(tile_key)
    )
    recv = lax.all_to_all(send, "pair", split_axis=0, concat_axis=0, tiled=True)
    recv_keys = lax.all_to_all(send_keys, "pair", split_axis=0, concat_axis=0, tiled=True)
    arrived = recv.reshape(owner_count * capacity, TS * TS)
    flat_keys = recv_keys.reshape(owner_count * capacity)
    row_block = flat_keys // NS
    col_block = flat_keys % NS
    places = jnp.arange(ROWSETS_DEV * NS, dtype=jnp.int32)
    chooser = (places[:, None] == flat_keys[None, :]).astype(jnp.float32)
    stacked = jnp.dot(
        chooser, arrived, precision=lax.Precision.HIGHEST, preferred_element_type=jnp.float32
    )
    blocked = stacked.reshape(ROWSETS_DEV, NS, TS, TS).transpose(0, 2, 1, 3)
    blocked = blocked.reshape(ROWSETS_DEV * TS, NS * TS)
    product = jnp.dot(
        blocked,
        lax.all_gather(integrals, "vir", axis=0, tiled=True),
        precision=lax.Precision.HIGH,
        preferred_element_type=jnp.float32,
    )
    pairs = product.reshape(ROWSETS_DEV, TS, NS // 2, 2 * TS)[row_block, :, col_block // 2, :]
    answers = jnp.where(
        (col_block % 2 == 0)[:, None, None], pairs[:, :, :TS], pairs[:, :, TS:]
    ).reshape(owner_count, capacity, TS * TS)
    returned = lax.all_to_all(answers, "pair", split_axis=0, concat_axis=0, tiled=True)
    returned = returned.reshape(owner_count * capacity, TS * TS)
    return jnp.dot(
        packer.T, returned, precision=lax.Precision.HIGHEST, preferred_element_type=jnp.float32
    )


def solution(mesh):
    placed = (P(("pair", "vir"), None), P("vir", None), P(("pair", "vir")), P(("pair", "vir")))
    return jax.shard_map(
        per_device, mesh=mesh, in_specs=placed, out_specs=P(("pair", "vir"), None), check_vma=False
    )
```

```python
import jax
import jax.numpy as jnp
from jax import lax
from jax.sharding import PartitionSpec as P

TS = 64
NS = 24
ROWSETS_DEV = 24


def per_device(amplitudes, integrals, tile_owner, tile_key):
    owner_count = lax.axis_size("pair")
    capacity = max(2, 2 * amplitudes.shape[0] // owner_count)
    picked = (tile_owner[:, None] == jnp.arange(owner_count, dtype=jnp.int32)[None, :]).astype(
        jnp.int32
    )
    before = jnp.cumsum(picked, axis=0) - picked
    slot_index = jnp.sum(before * picked, axis=1)
    slots = jnp.arange(owner_count * capacity, dtype=jnp.int32)
    packer = (slots[:, None] == (tile_owner * capacity + slot_index)[None, :]).astype(jnp.float32)
    send = jnp.dot(
        packer, amplitudes, precision=lax.Precision.HIGHEST, preferred_element_type=jnp.float32
    ).reshape(owner_count, capacity, TS * TS)
    send_keys = (
        jnp.zeros((owner_count, capacity), jnp.int32).at[tile_owner, slot_index].set(tile_key)
    )
    recv = lax.all_to_all(send, "pair", split_axis=0, concat_axis=0, tiled=True)
    recv_keys = lax.all_to_all(send_keys, "pair", split_axis=0, concat_axis=0, tiled=True)
    arrived = recv.reshape(owner_count * capacity, TS * TS)
    flat_keys = recv_keys.reshape(owner_count * capacity)
    row_block = flat_keys // NS
    col_block = flat_keys % NS
    tiles = arrived.reshape(owner_count * capacity, TS, TS)
    empty = jnp.zeros_like(tiles)
    odd = (col_block % 2 == 1)[:, None, None]
    halves = jnp.concatenate(
        [jnp.where(odd, empty, tiles), jnp.where(odd, tiles, empty)], axis=2
    ).reshape(owner_count * capacity, TS * 2 * TS)
    places = jnp.arange(ROWSETS_DEV * NS // 2, dtype=jnp.int32)
    chooser = (places[:, None] == (row_block * (NS // 2) + col_block // 2)[None, :]).astype(
        jnp.float32
    )
    stacked = jnp.dot(
        chooser, halves, precision=lax.Precision.HIGHEST, preferred_element_type=jnp.float32
    )
    blocked = stacked.reshape(ROWSETS_DEV, NS // 2, TS, 2 * TS).transpose(0, 2, 1, 3)
    right = lax.all_gather(integrals, "vir", axis=0, tiled=True).reshape(NS // 2, 2 * TS, NS * TS)
    product = lax.dot_general(
        blocked,
        right,
        (((2, 3), (0, 1)), ((), ())),
        precision=lax.Precision.HIGH,
        preferred_element_type=jnp.float32,
    )
    pairs = product.reshape(ROWSETS_DEV, TS, NS // 2, 2 * TS)[row_block, :, col_block // 2, :]
    answers = jnp.where(
        (col_block % 2 == 0)[:, None, None], pairs[:, :, :TS], pairs[:, :, TS:]
    ).reshape(owner_count, capacity, TS * TS)
    returned = lax.all_to_all(answers, "pair", split_axis=0, concat_axis=0, tiled=True)
    returned = returned.reshape(owner_count * capacity, TS * TS)
    return jnp.dot(
        packer.T, returned, precision=lax.Precision.HIGHEST, preferred_element_type=jnp.float32
    )


def solution(mesh):
    placed = (P(("pair", "vir"), None), P("vir", None), P(("pair", "vir")), P(("pair", "vir")))
    return jax.shard_map(
        per_device, mesh=mesh, in_specs=placed, out_specs=P(("pair", "vir"), None), check_vma=False
    )
```

```python
import jax
import jax.numpy as jnp
from jax import lax
from jax.sharding import PartitionSpec as P

TS = 64
NS = 24
ROWSETS_DEV = 24


def per_device(amplitudes, integrals, tile_owner, tile_key):
    owner_count = lax.axis_size("pair")
    capacity = max(2, 2 * amplitudes.shape[0] // owner_count)
    picked = (tile_owner[:, None] == jnp.arange(owner_count, dtype=jnp.int32)[None, :]).astype(
        jnp.int32
    )
    before = jnp.cumsum(picked, axis=0) - picked
    slot_index = jnp.sum(before * picked, axis=1)
    slots = jnp.arange(owner_count * capacity, dtype=jnp.int32)
    packer = (slots[:, None] == (tile_owner * capacity + slot_index)[None, :]).astype(jnp.float32)
    key_lanes = jnp.broadcast_to(tile_key.astype(jnp.float32)[:, None], (tile_key.shape[0], 128))
    payload = jnp.concatenate([amplitudes, key_lanes], axis=1)
    send = jnp.dot(
        packer, payload, precision=lax.Precision.HIGHEST, preferred_element_type=jnp.float32
    ).reshape(owner_count, capacity, TS * TS + 128)
    recv = lax.all_to_all(send, "pair", split_axis=0, concat_axis=0, tiled=True)
    recv = recv.reshape(owner_count * capacity, TS * TS + 128)
    arrived = recv[:, : TS * TS]
    flat_keys = recv[:, TS * TS].astype(jnp.int32)
    row_block = flat_keys // NS
    col_block = flat_keys % NS
    tiles = arrived.reshape(owner_count * capacity, TS, TS)
    empty = jnp.zeros_like(tiles)
    odd = (col_block % 2 == 1)[:, None, None]
    halves = jnp.concatenate(
        [jnp.where(odd, empty, tiles), jnp.where(odd, tiles, empty)], axis=2
    ).reshape(owner_count * capacity, TS * 2 * TS)
    places = jnp.arange(ROWSETS_DEV * NS // 2, dtype=jnp.int32)
    chooser = (places[:, None] == (row_block * (NS // 2) + col_block // 2)[None, :]).astype(
        jnp.float32
    )
    stacked = jnp.dot(
        chooser, halves, precision=lax.Precision.HIGHEST, preferred_element_type=jnp.float32
    )
    blocked = stacked.reshape(ROWSETS_DEV, NS // 2, TS, 2 * TS).transpose(0, 2, 1, 3)
    right = lax.all_gather(integrals, "vir", axis=0, tiled=True).reshape(NS // 2, 2 * TS, NS * TS)
    product = lax.dot_general(
        blocked,
        right,
        (((2, 3), (0, 1)), ((), ())),
        precision=lax.Precision.HIGH,
        preferred_element_type=jnp.float32,
    )
    pairs = product.reshape(ROWSETS_DEV, TS, NS // 2, 2 * TS)[row_block, :, col_block // 2, :]
    answers = jnp.where(
        (col_block % 2 == 0)[:, None, None], pairs[:, :, :TS], pairs[:, :, TS:]
    ).reshape(owner_count, capacity, TS * TS)
    returned = lax.all_to_all(answers, "pair", split_axis=0, concat_axis=0, tiled=True)
    returned = returned.reshape(owner_count * capacity, TS * TS)
    return jnp.dot(
        packer.T, returned, precision=lax.Precision.HIGHEST, preferred_element_type=jnp.float32
    )


def solution(mesh):
    placed = (P(("pair", "vir"), None), P("vir", None), P(("pair", "vir")), P(("pair", "vir")))
    return jax.shard_map(
        per_device, mesh=mesh, in_specs=placed, out_specs=P(("pair", "vir"), None), check_vma=False
    )
```

```python
import jax
import jax.numpy as jnp
from jax import lax
from jax.sharding import PartitionSpec as P

TS = 64
NS = 24
ROWSETS_DEV = 24


def per_device(amplitudes, integrals, tile_owner, tile_key):
    owner_count = lax.axis_size("pair")
    capacity = max(2, 2 * amplitudes.shape[0] // owner_count)
    picked = (tile_owner[:, None] == jnp.arange(owner_count, dtype=jnp.int32)[None, :]).astype(
        jnp.int32
    )
    before = jnp.cumsum(picked, axis=0) - picked
    slot_index = jnp.sum(before * picked, axis=1)
    slots = jnp.arange(owner_count * capacity, dtype=jnp.int32)
    packer = (slots[:, None] == (tile_owner * capacity + slot_index)[None, :]).astype(jnp.float32)
    key_lanes = jnp.broadcast_to(tile_key.astype(jnp.float32)[:, None], (tile_key.shape[0], 128))
    payload = jnp.concatenate([amplitudes, key_lanes], axis=1)
    send = jnp.dot(
        packer, payload, precision=lax.Precision.HIGHEST, preferred_element_type=jnp.float32
    ).reshape(owner_count, capacity, TS * TS + 128)
    recv = lax.all_to_all(send, "pair", split_axis=0, concat_axis=0, tiled=True)
    recv = recv.reshape(owner_count * capacity, TS * TS + 128)
    arrived = recv[:, : TS * TS]
    flat_keys = recv[:, TS * TS].astype(jnp.int32)
    row_block = flat_keys // NS
    col_block = flat_keys % NS
    tiles = arrived.reshape(owner_count * capacity, TS, TS)
    empty = jnp.zeros_like(tiles)
    odd = (col_block % 2 == 1)[:, None, None]
    halves = jnp.concatenate(
        [jnp.where(odd, empty, tiles), jnp.where(odd, tiles, empty)], axis=2
    ).reshape(owner_count * capacity, TS * 2 * TS)
    places = jnp.arange(ROWSETS_DEV * NS // 2, dtype=jnp.int32)
    chooser = (places[:, None] == (row_block * (NS // 2) + col_block // 2)[None, :]).astype(
        jnp.float32
    )
    stacked = jnp.dot(
        chooser, halves, precision=lax.Precision.HIGH, preferred_element_type=jnp.float32
    )
    blocked = stacked.reshape(ROWSETS_DEV, NS // 2, TS, 2 * TS).transpose(0, 2, 1, 3)
    right = lax.all_gather(integrals, "vir", axis=0, tiled=True).reshape(NS // 2, 2 * TS, NS * TS)
    product = lax.dot_general(
        blocked,
        right,
        (((2, 3), (0, 1)), ((), ())),
        precision=lax.Precision.HIGH,
        preferred_element_type=jnp.float32,
    )
    pairs = product.reshape(ROWSETS_DEV, TS, NS // 2, 2 * TS)[row_block, :, col_block // 2, :]
    answers = jnp.where(
        (col_block % 2 == 0)[:, None, None], pairs[:, :, :TS], pairs[:, :, TS:]
    ).reshape(owner_count, capacity, TS * TS)
    returned = lax.all_to_all(answers, "pair", split_axis=0, concat_axis=0, tiled=True)
    returned = returned.reshape(owner_count * capacity, TS * TS)
    return jnp.dot(
        packer.T, returned, precision=lax.Precision.HIGHEST, preferred_element_type=jnp.float32
    )


def solution(mesh):
    placed = (P(("pair", "vir"), None), P("vir", None), P(("pair", "vir")), P(("pair", "vir")))
    return jax.shard_map(
        per_device, mesh=mesh, in_specs=placed, out_specs=P(("pair", "vir"), None), check_vma=False
    )
```

```python
import jax
import jax.numpy as jnp
from jax import lax
from jax.sharding import PartitionSpec as P

TS = 64
NS = 24
ROWSETS_DEV = 24


def per_device(amplitudes, integrals, tile_owner, tile_key):
    owner_count = lax.axis_size("pair")
    capacity = max(2, 2 * amplitudes.shape[0] // owner_count)
    picked = (tile_owner[:, None] == jnp.arange(owner_count, dtype=jnp.int32)[None, :]).astype(
        jnp.int32
    )
    before = jnp.cumsum(picked, axis=0) - picked
    slot_index = jnp.sum(before * picked, axis=1)
    slots = jnp.arange(owner_count * capacity, dtype=jnp.int32)
    packer = (slots[:, None] == (tile_owner * capacity + slot_index)[None, :]).astype(jnp.float32)
    key_lanes = jnp.broadcast_to(tile_key.astype(jnp.float32)[:, None], (tile_key.shape[0], 128))
    payload = jnp.concatenate([amplitudes, key_lanes], axis=1)
    send = jnp.dot(
        packer, payload, precision=lax.Precision.HIGHEST, preferred_element_type=jnp.float32
    ).reshape(owner_count, capacity, TS * TS + 128)
    recv = lax.all_to_all(send, "pair", split_axis=0, concat_axis=0, tiled=True)
    recv = recv.reshape(owner_count * capacity, TS * TS + 128)
    arrived = recv[:, : TS * TS]
    flat_keys = recv[:, TS * TS].astype(jnp.int32)
    row_block = flat_keys // NS
    col_block = flat_keys % NS
    tiles = arrived.reshape(owner_count * capacity, TS, 1, TS)
    side = (jnp.arange(2, dtype=jnp.int32)[None, :] == (col_block % 2)[:, None])[:, None, :, None]
    halves = jnp.where(side, tiles, 0.0).reshape(owner_count * capacity, TS * 2 * TS)
    places = jnp.arange(ROWSETS_DEV * NS // 2, dtype=jnp.int32)
    chooser = (places[:, None] == (row_block * (NS // 2) + col_block // 2)[None, :]).astype(
        jnp.float32
    )
    stacked = jnp.dot(
        chooser, halves, precision=lax.Precision.HIGH, preferred_element_type=jnp.float32
    )
    blocked = stacked.reshape(ROWSETS_DEV, NS // 2, TS, 2 * TS).transpose(0, 2, 1, 3)
    right = lax.all_gather(integrals, "vir", axis=0, tiled=True).reshape(NS // 2, 2 * TS, NS * TS)
    product = lax.dot_general(
        blocked,
        right,
        (((2, 3), (0, 1)), ((), ())),
        precision=lax.Precision.HIGH,
        preferred_element_type=jnp.float32,
    )
    pairs = product.reshape(ROWSETS_DEV, TS, NS // 2, 2 * TS)[row_block, :, col_block // 2, :]
    answers = jnp.where(
        (col_block % 2 == 0)[:, None, None], pairs[:, :, :TS], pairs[:, :, TS:]
    ).reshape(owner_count, capacity, TS * TS)
    returned = lax.all_to_all(answers, "pair", split_axis=0, concat_axis=0, tiled=True)
    returned = returned.reshape(owner_count * capacity, TS * TS)
    return jnp.dot(
        packer.T, returned, precision=lax.Precision.HIGHEST, preferred_element_type=jnp.float32
    )


def solution(mesh):
    placed = (P(("pair", "vir"), None), P("vir", None), P(("pair", "vir")), P(("pair", "vir")))
    return jax.shard_map(
        per_device, mesh=mesh, in_specs=placed, out_specs=P(("pair", "vir"), None), check_vma=False
    )
```

```python
import jax
import jax.numpy as jnp
from jax import lax
from jax.sharding import PartitionSpec as P

TS = 64
NS = 24
ROWSETS_DEV = 24


def per_device(amplitudes, integrals, tile_owner, tile_key):
    owner_count = lax.axis_size("pair")
    capacity = max(2, 2 * amplitudes.shape[0] // owner_count)
    picked = (tile_owner[:, None] == jnp.arange(owner_count, dtype=jnp.int32)[None, :]).astype(
        jnp.int32
    )
    before = jnp.cumsum(picked, axis=0) - picked
    slot_index = jnp.sum(before * picked, axis=1)
    slots = jnp.arange(owner_count * capacity, dtype=jnp.int32)
    packer = (slots[:, None] == (tile_owner * capacity + slot_index)[None, :]).astype(jnp.float32)
    key_lanes = jnp.broadcast_to(tile_key.astype(jnp.float32)[:, None], (tile_key.shape[0], 128))
    payload = jnp.concatenate([amplitudes, key_lanes], axis=1)
    send = jnp.dot(
        packer, payload, precision=lax.Precision.HIGH, preferred_element_type=jnp.float32
    ).reshape(owner_count, capacity, TS * TS + 128)
    recv = lax.all_to_all(send, "pair", split_axis=0, concat_axis=0, tiled=True)
    recv = recv.reshape(owner_count * capacity, TS * TS + 128)
    arrived = recv[:, : TS * TS]
    flat_keys = recv[:, TS * TS].astype(jnp.int32)
    row_block = flat_keys // NS
    col_block = flat_keys % NS
    tiles = arrived.reshape(owner_count * capacity, TS, 1, TS)
    side = (jnp.arange(2, dtype=jnp.int32)[None, :] == (col_block % 2)[:, None])[:, None, :, None]
    halves = jnp.where(side, tiles, 0.0).reshape(owner_count * capacity, TS * 2 * TS)
    places = jnp.arange(ROWSETS_DEV * NS // 2, dtype=jnp.int32)
    chooser = (places[:, None] == (row_block * (NS // 2) + col_block // 2)[None, :]).astype(
        jnp.float32
    )
    stacked = jnp.dot(
        chooser, halves, precision=lax.Precision.HIGH, preferred_element_type=jnp.float32
    )
    blocked = stacked.reshape(ROWSETS_DEV, NS // 2, TS, 2 * TS).transpose(0, 2, 1, 3)
    right = lax.all_gather(integrals, "vir", axis=0, tiled=True).reshape(NS // 2, 2 * TS, NS * TS)
    product = lax.dot_general(
        blocked,
        right,
        (((2, 3), (0, 1)), ((), ())),
        precision=lax.Precision.HIGH,
        preferred_element_type=jnp.float32,
    )
    pairs = product.reshape(ROWSETS_DEV, TS, NS // 2, 2 * TS)[row_block, :, col_block // 2, :]
    answers = jnp.where(
        (col_block % 2 == 0)[:, None, None], pairs[:, :, :TS], pairs[:, :, TS:]
    ).reshape(owner_count, capacity, TS * TS)
    returned = lax.all_to_all(answers, "pair", split_axis=0, concat_axis=0, tiled=True)
    returned = returned.reshape(owner_count * capacity, TS * TS)
    return jnp.dot(
        packer.T, returned, precision=lax.Precision.HIGH, preferred_element_type=jnp.float32
    )


def solution(mesh):
    placed = (P(("pair", "vir"), None), P("vir", None), P(("pair", "vir")), P(("pair", "vir")))
    return jax.shard_map(
        per_device, mesh=mesh, in_specs=placed, out_specs=P(("pair", "vir"), None), check_vma=False
    )
```
